32 devices in a mesh: pipe: 4 (over x, core), tensor: 8 (over z, y).
Axes of the slice: x: 2, y: 2, z: 4, core: 2. Of those that a mesh axis runs over, the one named last changes fastest.
Arguments:
- stretch: bfloat16 [768, 7168], P(('pipe', 'tensor')), may hold values from -6 to 6
- ln_gain: float32 [7168], replicated, may hold values from 0.5 to 1.5
- ln_bias: float32 [7168], replicated, may hold values from -1.75 to 1.75
- qkv_weight: bfloat16 [7168, 12288], P(None, 'tensor'), may hold values from -0.0625 to 0.0625
- qkv_bias: float32 [12288], P('tensor'), may hold values from -1.75 to 1.75
- out_weight: bfloat16 [4096, 7168], P('tensor'), may hold values from -0.09375 to 0.09375
- out_bias: float32 [7168], replicated, may hold values from -1.75 to 1.75
- segment_ids: int32 [768], P('pipe'), may hold values from 0 to 31, never falling along the last dimension, each value on 1 to 96 neighbouring positions
- prefill_cache: bfloat16 [1, 32, 2, 128, 4096], P(None, ('pipe', 'tensor')), may hold values from -6 to 6
- block_dest: int32 [1, 32, 1], P(None, 'pipe'), may hold values from 0 to 3; in each aligned block of 8 rows (0 to 7, 8 to 15, ..., all dimensions but the last counted through in order) at most 3 rows name the same one
Outputs:
- mixed: bfloat16 [768, 7168], P(('pipe', 'tensor'))
- decode_side_cache: bfloat16 [1, 48, 2, 128, 4096], P(None, 'pipe', None, None, 'tensor')
The draws below stay inside these ranges and needn't reach their ends.
Inputs may be any that keep to these rules, and one draw needn't show every extreme that they name: `block_dest`: among the 8 blocks of one group and one layer no decode group is named more than 3 times, and some decode group exactly 3 times. `segment_ids`: never falling along the tokens; a request spans at most 96 tokens.
All inputs are finite; a program needn't handle non-finite values.
Results may differ from the reference program's by a relative error of at most 0.013.
Values may be sent and summed in bfloat16 or wider, within the bound.
No kernel may reach another device: no remote copies, remote signals or barrier semaphores. Data moves between devices by JAX's collectives and lax.ppermute only.
A program may use at most 128 MiB of HBM per device.

```python
import math
import jax
import jax.numpy as jnp
import numpy as np
from jax import lax

D = 7168
HEADS = 32
HD = 128
CL = 1
BLK = 128
TOKENS = 192
ALLTOK = 768
ROWBLK = 8
PRE = 1024
NBLK = 32
CAP = 3
SEGS = 32
N_PIPE = 4


def shard_levels(rng, shape, shards, least, high):
    level = 1.0
    for dim, parts in shards:
        heights = jax.random.uniform(jax.random.fold_in(jax.random.fold_in(rng, 6), dim), (parts,), jnp.float32, least / len(shards), high / len(shards))
        level = level * jnp.repeat(jnp.exp(heights), shape[dim] // parts).reshape((-1,) + (1,) * (len(shape) - 1 - dim))
    return level


def split_up(number_of, total, reach, skew):
    loads = [(1 << 20) // math.isqrt(rank ** skew) + 1 for rank in range(2, number_of + 1)]
    spare, counts = total - reach - (number_of - 1), [1] * (number_of - 1)
    while spare > 0:
        movable = [i for i in range(number_of - 1) if counts[i] < reach]
        pool, remaining = sum([loads[i] for i in movable]), spare
        for i in movable:
            more = min(reach - counts[i], max(1, remaining * loads[i] // pool), spare)
            counts[i] = counts[i] + more
            spare = spare - more
    return np.array([reach] + counts)


def ragged(key, number_of, total, limit, lean):
    if number_of == 2:
        one = jax.random.randint(key, (), max(1, total - limit), min(limit, total - 1) + 1)
        return jnp.stack([one, total - one])
    lengths = jnp.asarray(split_up(number_of, total, limit, lean), jnp.int32)
    pairs = (number_of - 1) // 2
    giver, taker = lengths[1:1 + 2 * pairs:2], lengths[2:2 + 2 * pairs:2]
    room = jnp.minimum(giver - 1, limit - taker)
    shifted = jax.random.randint(jax.random.fold_in(key, 1), (pairs,), 0, 1 << 20) % (room + 1)
    lengths = lengths.at[1:1 + 2 * pairs:2].set(giver - shifted).at[2:2 + 2 * pairs:2].set(taker + shifted)
    return lengths[jax.random.permutation(jax.random.fold_in(key, 2), number_of)]


def assign_block(rng, own, number, rows, amount, top, most, slope):
    order = jax.random.permutation(rng, amount)
    heavy_load, usual = shares(amount, rows * top, most, slope, True), shares(amount, rows * top, most, slope, False)
    places = jnp.arange(amount)

    def named(sizes, turn):
        used = int((sizes > 0).sum())
        fixed = max(1, used // 4)
        shifted = fixed + (places - fixed + turn * (used - fixed)) % max(1, amount - fixed)
        return jnp.zeros((amount,), jnp.int32).at[order[jnp.where(places < fixed, places, shifted)]].set(jnp.asarray(sizes, jnp.int32))

    sizes = jnp.where(number % 4 == 0, named(heavy_load, number // 4), named(usual, number - number // 4 - 1))
    mixed = jax.random.permutation(jax.random.fold_in(own, 3), amount)
    giver, receiver = mixed[0:amount // 2 * 2:2], mixed[1:amount // 2 * 2:2]
    slack = jnp.minimum(sizes[giver] - 1, most - sizes[receiver]) // 2
    slack = jnp.where((giver == order[0]) | (receiver == order[0]) | (sizes[receiver] == 0), 0, jnp.maximum(slack, 0))
    shifted = jax.random.randint(jax.random.fold_in(own, 4), (amount // 2,), 0, 1 << 20) % (slack + 1)
    sizes = sizes.at[giver].add(-shifted).at[receiver].add(shifted)
    members = jnp.searchsorted(jnp.cumsum(sizes), jnp.arange(rows * top), side="right").astype(jnp.int32)
    listing = members.reshape(top, rows).T
    listing = listing[jax.random.permutation(jax.random.fold_in(own, 1), rows)]
    turn = jax.random.randint(jax.random.fold_in(own, 2), (rows, 1), 0, top)
    return jnp.take_along_axis(listing, (jnp.arange(top)[None, :] + turn) % top, axis=1)


def shares(number_of, total, reach, skew, full):
    weights = [(1 << 20) // math.isqrt(rank ** skew) + 1 for rank in range(1, number_of + 1)]
    largest = reach if full else min(reach, max(-(-total // number_of), total * weights[0] // sum(weights)))
    least = 1 if total - largest >= number_of - 1 else 0
    given, rest = [largest] + [least] * (number_of - 1), total - largest - least * (number_of - 1)
    while rest > 0:
        candidates = [i for i in range(1, number_of) if given[i] < largest] or [i for i in range(1, number_of) if given[i] < reach]
        mass, budget = sum([weights[i] for i in candidates]), rest
        for i in candidates:
            addition = min(reach - given[i], max(1, budget * weights[i] // mass), rest)
            given[i] = given[i] + addition
            rest = rest - addition
    return np.array(given)


def normal_values(key, dims, width, most, shards=(), held_as=jnp.bfloat16):
    result = jax.random.normal(key, dims, jnp.float32) * width
    if len(shards) > 0:
        result = shard_levels(key, dims, shards, -0.22, 0.18) * result
    return jnp.clip(result, min=-most, max=most).astype(held_as)


def setup_inputs(seed: int = 0) -> dict:
    key_of = jax.random.split(jax.random.key(seed), 11)
    stretch = normal_values(key_of[0], (ALLTOK, D), 1.0, 6.0, ((0, 32),))
    ln_gain = jnp.clip(1.0 + 0.1 * jax.random.normal(key_of[1], (D,), jnp.float32), 0.5, 1.5)
    ln_bias = normal_values(key_of[2], (D,), 0.3, 1.75, (), jnp.float32)
    qkv_weight = normal_values(key_of[3], (D, HEADS * 3 * HD), D ** -0.5, 0.0625, ((1, 8),))
    qkv_bias = normal_values(key_of[4], (HEADS * 3 * HD,), 0.3, 1.75, ((0, 8),), jnp.float32)
    out_weight = normal_values(key_of[5], (HEADS * HD, D), (HEADS * HD) ** -0.5, 0.09375, ((0, 8),))
    out_bias = normal_values(key_of[6], (D,), 0.3, 1.75, (), jnp.float32)
    segment_ids = jnp.searchsorted(jnp.cumsum(ragged(key_of[7], SEGS, ALLTOK, TOKENS // 2, 2)), jnp.arange(ALLTOK), side="right").astype(jnp.int32)
    prefill_cache = normal_values(key_of[8], (CL, NBLK, 2, BLK, HEADS * HD), 1.0, 6.0, ((1, 32),))
    block_dest_keys = jax.random.split(jax.random.fold_in(key_of[9], 1), CL * NBLK // ROWBLK)
    block_dest_turns = jax.random.permutation(jax.random.fold_in(key_of[9], 3), CL * NBLK // ROWBLK)
    block_dest = jax.vmap(lambda own, number: assign_block(jax.random.fold_in(key_of[9], 2), own, number, ROWBLK, N_PIPE, 1, CAP, 2))(block_dest_keys, block_dest_turns).reshape((CL, NBLK, 1))
    return {"stretch": stretch, "ln_gain": ln_gain, "ln_bias": ln_bias, "qkv_weight": qkv_weight, "qkv_bias": qkv_bias, "out_weight": out_weight, "out_bias": out_bias, "segment_ids": segment_ids, "prefill_cache": prefill_cache, "block_dest": block_dest}


def normalize(x, gain, shift):
    mean = lax.optimization_barrier(jnp.mean(x, axis=-1, keepdims=True))
    var = lax.optimization_barrier(jnp.mean((x - mean) * (x - mean), axis=-1, keepdims=True))
    return ((x - mean) * lax.rsqrt(var + 1e-05) * gain + shift).astype(jnp.bfloat16)

def group_attention(packed):
    qkv, segs, finished = packed
    heads = qkv.reshape(TOKENS, HEADS, 3, HD).astype(jnp.float32)
    query = heads[:, :, 0]
    keys = heads[:, :, 1]
    value_rows = heads[:, :, 2]
    cached_keys = finished[:, 0].reshape(PRE, HEADS, HD).astype(jnp.float32)
    old_values = finished[:, 1].reshape(PRE, HEADS, HD).astype(jnp.float32)
    all_keys = jnp.concatenate([cached_keys, keys], axis=0)
    all_values = jnp.concatenate([old_values, value_rows], axis=0)
    scores = jnp.einsum('qhd,khd->hqk', query, all_keys) * HD ** (-0.5)
    place = jnp.arange(TOKENS)
    own_visible = (segs[:, None] == segs[None, :]) & (place[None, :] <= place[:, None])
    old_visible = jnp.broadcast_to((segs == segs[0])[:, None], (TOKENS, PRE))
    visible = jnp.concatenate([old_visible, own_visible], axis=1)
    scores = jnp.where(visible[None], scores, -jnp.inf)
    weights = jax.nn.softmax(scores, axis=-1).astype(jnp.bfloat16)
    context = jnp.einsum('hqk,khd->qhd', weights.astype(jnp.float32), all_values)
    return context.reshape(TOKENS, HEADS * HD).astype(jnp.bfloat16)

def reference(stretch, ln_gain, ln_bias, qkv_weight, qkv_bias, out_weight, out_bias, segment_ids, prefill_cache, block_dest):
    hidden = stretch.astype(jnp.float32)
    normed = normalize(hidden, ln_gain, ln_bias)
    qkv = (jnp.dot(normed, qkv_weight, preferred_element_type=jnp.float32) + qkv_bias).astype(jnp.bfloat16)
    finished = prefill_cache[0].reshape(N_PIPE, ROWBLK, 2, BLK, HEADS * HD)
    finished = jnp.transpose(finished, (0, 1, 3, 2, 4)).reshape(N_PIPE, PRE, 2, HEADS * HD)
    context = lax.map(group_attention, (qkv.reshape(N_PIPE, TOKENS, HEADS * 3 * HD), segment_ids.reshape(N_PIPE, TOKENS), finished))
    context = context.reshape(ALLTOK, HEADS * HD)
    mixed = (hidden + jnp.dot(context, out_weight, preferred_element_type=jnp.float32) + out_bias).astype(jnp.bfloat16)
    layers = []
    for layer in range(CL):
        dest = block_dest[layer, :, 0].astype(jnp.int32)
        onehot = (dest[:, None] == jnp.arange(N_PIPE, dtype=jnp.int32)[None, :]).astype(jnp.int32)
        grouped = onehot.reshape(N_PIPE, ROWBLK, N_PIPE)
        earlier_tokens = jnp.cumsum(grouped, axis=1) - grouped
        slot = lax.optimization_barrier(jnp.sum(earlier_tokens * grouped, axis=-1)).reshape(NBLK)
        source = jnp.arange(NBLK, dtype=jnp.int32) // ROWBLK
        position = dest * (N_PIPE * CAP) + source * CAP + slot
        placed_blocks = jnp.zeros((N_PIPE * N_PIPE * CAP, 2, BLK, HEADS * HD), jnp.bfloat16)
        layers.append(placed_blocks.at[position].set(prefill_cache[layer]))
    return (mixed, jnp.stack(layers, axis=0))
```

```python
import jax
import jax.numpy as jnp
from jax import lax
from jax.sharding import PartitionSpec as P

HD = 128
PIPE_PERMUTE = True
A2A_PERMUTE = True
RELAY_BARRIER = True


def normalize(x, gain, shift):
    mean = jnp.mean(x, axis=-1, keepdims=True)
    var = jnp.mean((x - mean) * (x - mean), axis=-1, keepdims=True)
    return ((x - mean) * lax.rsqrt(var + 1e-05) * gain + shift).astype(jnp.bfloat16)


def shifted(x, axis, k, n):
    return lax.ppermute(x, axis, [(j, (j + k) % n) for j in range(n)])


def gather_heads(prefill_cache):
    tensor_count = lax.axis_size("tensor")
    if not A2A_PERMUTE:
        rows = lax.all_to_all(prefill_cache, "tensor", split_axis=4, concat_axis=1, tiled=True)
        return rows, jnp.arange(tensor_count)
    i = lax.axis_index("tensor")
    layers, _, two, blk, width = prefill_cache.shape
    chunks = prefill_cache.reshape(layers, two, blk, tensor_count, width // tensor_count)
    arrived = []
    for k in range(tensor_count):
        piece = lax.dynamic_index_in_dim(chunks, (i + k) % tensor_count, 3, keepdims=False)
        arrived.append(piece if k == 0 else shifted(piece, "tensor", k, tensor_count))
    rows = jnp.stack(arrived, axis=1)
    return rows, (i - jnp.arange(tensor_count)) % tensor_count


def send_decode(per_head_rows, block_of, block_dest):
    layers = per_head_rows.shape[0]
    pipe_count = lax.axis_size("pipe")
    row_blocks = per_head_rows.shape[1]
    capacity = 3 * row_blocks // (2 * pipe_count)
    dest = block_dest[:, :, 0]
    onehot = (dest[:, :, None] == jnp.arange(pipe_count, dtype=jnp.int32)[None, None, :]).astype(
        jnp.int32
    )
    earlier_tokens = jnp.cumsum(onehot, axis=1) - onehot
    slot = jnp.sum(earlier_tokens * onehot, axis=-1)
    position = (dest * capacity + slot)[:, block_of]
    targets = jnp.arange(pipe_count * capacity, dtype=jnp.int32)
    placement_index = (position[:, None, :] == targets[None, :, None]).astype(jnp.bfloat16)
    outgoing = jnp.einsum(
        "gud,gdoih->guoih", placement_index, per_head_rows, preferred_element_type=jnp.float32
    ).astype(jnp.bfloat16)
    outgoing = outgoing.reshape((layers, pipe_count, capacity) + per_head_rows.shape[2:])
    if not PIPE_PERMUTE:
        arrived = lax.all_to_all(outgoing, "pipe", split_axis=1, concat_axis=1, tiled=True)
        return arrived.reshape((layers, pipe_count * capacity) + per_head_rows.shape[2:])
    i = lax.axis_index("pipe")
    arrived = []
    for k in range(pipe_count):
        piece = lax.dynamic_index_in_dim(outgoing, (i + k) % pipe_count, 1, keepdims=False)
        arrived.append(piece if k == 0 else shifted(piece, "pipe", k, pipe_count))
    arrived = jnp.stack(arrived, axis=1)
    arrived = jnp.take(arrived, (i - jnp.arange(pipe_count)) % pipe_count, axis=1)
    return arrived.reshape((layers, pipe_count * capacity) + per_head_rows.shape[2:])


def partner(x):
    tensor_count = lax.axis_size("tensor")
    return lax.ppermute(x, "tensor", [(j, j ^ 1) for j in range(tensor_count)])


def ring(x):
    tensor_count = lax.axis_size("tensor")
    rows = tensor_count // 2
    return lax.ppermute(
        x, "tensor", [(j, ((j // 2 + 1) % rows) * 2 + j % 2) for j in range(tensor_count)]
    )


def gather_tokens(x):
    tensor_count = lax.axis_size("tensor")
    rows = tensor_count // 2
    i = lax.axis_index("tensor")
    outer, inner = i // 2, i % 2
    own = [x]
    for _ in range(1, rows):
        own.append(ring(own[-1]))
    other = [partner(piece) for piece in own]
    steps = jnp.arange(rows)
    source = jnp.concatenate(
        [((outer - steps) % rows) * 2 + inner, ((outer - steps) % rows) * 2 + (1 - inner)]
    )
    return jnp.concatenate(own + other, axis=0), source


def scatter_tokens(partial):
    tensor_count = lax.axis_size("tensor")
    rows = tensor_count // 2
    blocks = partial.reshape((2, rows, -1) + partial.shape[1:])
    mine = [
        blocks[0, s] + partner(blocks[1, s].astype(jnp.bfloat16)).astype(jnp.float32)
        for s in range(rows)
    ]
    carried = mine[1 % rows]
    for k in range(1, rows):
        arrived = ring(carried.astype(jnp.bfloat16)).astype(jnp.float32)
        carried = arrived + mine[(k + 1) % rows]
    return carried


def local(
    stretch,
    ln_gain,
    ln_bias,
    qkv_weight,
    qkv_bias,
    out_weight,
    out_bias,
    segment_ids,
    prefill_cache,
    block_dest,
):
    per_head_rows, block_of = gather_heads(prefill_cache)
    decode_side_cache = send_decode(per_head_rows, block_of, block_dest)
    hidden = stretch.astype(jnp.float32)
    head_count = qkv_weight.shape[1] // (3 * HD)
    normed = normalize(hidden, ln_gain, ln_bias)
    gathered, source = gather_tokens(normed)
    qkv = (
        jnp.dot(gathered, qkv_weight, preferred_element_type=jnp.float32) + qkv_bias
    ).astype(jnp.bfloat16)
    group_tokens = qkv.shape[0]
    place = (source[:, None] * normed.shape[0] + jnp.arange(normed.shape[0])[None, :]).reshape(-1)
    first_segment = segment_ids[0]
    segment_ids = segment_ids[place]
    heads = qkv.reshape(group_tokens, head_count, 3, HD)
    query = heads[:, :, 0]
    keys = heads[:, :, 1]
    value_rows = heads[:, :, 2]
    finished = per_head_rows[0]
    prefix_length = finished.shape[0] * finished.shape[2]
    cached_keys = finished[:, 0].reshape(prefix_length, head_count, HD)
    old_values = finished[:, 1].reshape(prefix_length, head_count, HD)
    scale = HD ** (-0.5)
    own_scores = jnp.einsum("qhd,khd->hqk", query, keys, preferred_element_type=jnp.float32) * scale
    old_scores = (
        jnp.einsum("qhd,khd->hqk", query, cached_keys, preferred_element_type=jnp.float32) * scale
    )
    own_visible = (segment_ids[:, None] == segment_ids[None, :]) & (
        place[None, :] <= place[:, None]
    )
    old_visible = (segment_ids == first_segment)[:, None]
    own_scores = jnp.where(own_visible[None], own_scores, -jnp.inf)
    old_scores = jnp.where(old_visible[None], old_scores, -jnp.inf)
    scores = jnp.concatenate([old_scores, own_scores], axis=2)
    weights = jax.nn.softmax(scores, axis=-1).astype(jnp.bfloat16)
    context = jnp.einsum(
        "hqk,khd->qhd",
        weights[:, :, :prefix_length],
        old_values,
        preferred_element_type=jnp.float32,
    )
    context = context + jnp.einsum(
        "hqk,khd->qhd",
        weights[:, :, prefix_length:],
        value_rows,
        preferred_element_type=jnp.float32,
    )
    context = context.astype(jnp.bfloat16).reshape(group_tokens, head_count * HD)
    if RELAY_BARRIER:
        decode_side_cache, context = lax.optimization_barrier((decode_side_cache, context))
    summed = scatter_tokens(jnp.dot(context, out_weight, preferred_element_type=jnp.float32))
    mixed = (hidden + summed + out_bias).astype(jnp.bfloat16)
    return (mixed, decode_side_cache)


def solution(mesh):
    return jax.shard_map(
        local,
        mesh=mesh,
        in_specs=(
            P(("pipe", "tensor"), None),
            P(),
            P(),
            P(None, "tensor"),
            P("tensor"),
            P("tensor", None),
            P(),
            P("pipe"),
            P(None, ("pipe", "tensor"), None, None, None),
            P(None, "pipe", None),
        ),
        out_specs=(P(("pipe", "tensor"), None), P(None, "pipe", None, None, "tensor")),
        check_vma=False,
    )
```

```python
import jax
import jax.numpy as jnp
from jax import lax
from jax.sharding import PartitionSpec as P

HD = 128
RELAY_STEP = 3


def normalize(x, gain, shift):
    mean = jnp.mean(x, axis=-1, keepdims=True)
    var = jnp.mean((x - mean) * (x - mean), axis=-1, keepdims=True)
    return ((x - mean) * lax.rsqrt(var + 1e-05) * gain + shift).astype(jnp.bfloat16)


def shifted(x, axis, k, n):
    return lax.ppermute(x, axis, [(j, (j + k) % n) for j in range(n)])


def split_heads(prefill_cache):
    tensor_count = lax.axis_size("tensor")
    layers, _, two, blk, width = prefill_cache.shape
    local_heads = width // tensor_count // HD
    split = prefill_cache.reshape(layers, two, blk, tensor_count, local_heads, HD)
    return jnp.transpose(split, (0, 1, 4, 3, 2, 5))


def send_decode(per_head_rows, block_dest):
    layers, two, local_heads, row_blocks, blk, _ = per_head_rows.shape
    pipe_count = lax.axis_size("pipe")
    capacity = 3 * row_blocks // (2 * pipe_count)
    dest = block_dest[:, :, 0]
    onehot = (dest[:, :, None] == jnp.arange(pipe_count, dtype=jnp.int32)[None, None, :]).astype(
        jnp.int32
    )
    earlier_tokens = jnp.cumsum(onehot, axis=1) - onehot
    slot = jnp.sum(earlier_tokens * onehot, axis=-1)
    position = dest * capacity + slot
    i = lax.axis_index("pipe")
    outgoing = []
    for k in range(pipe_count):
        targets = ((i + k) % pipe_count) * capacity + jnp.arange(capacity, dtype=jnp.int32)
        placement_index = (position[:, None, :] == targets[None, :, None]).astype(jnp.bfloat16)
        piece = jnp.einsum(
            "gud,gohdtc->guothc", placement_index, per_head_rows, preferred_element_type=jnp.float32
        ).astype(jnp.bfloat16)
        outgoing.append(piece.reshape((layers, capacity, two, blk, local_heads * HD)))
    return outgoing


def receive_decode(outgoing):
    pipe_count = lax.axis_size("pipe")
    i = lax.axis_index("pipe")
    layers, capacity = outgoing[0].shape[:2]
    arrived = jnp.zeros((layers, pipe_count * capacity) + outgoing[0].shape[2:], outgoing[0].dtype)
    for k in range(pipe_count):
        piece = outgoing[k] if k == 0 else shifted(outgoing[k], "pipe", k, pipe_count)
        arrived = lax.dynamic_update_slice_in_dim(
            arrived, piece, ((i - k) % pipe_count) * capacity, axis=1
        )
    return arrived

def partner(x):
    tensor_count = lax.axis_size("tensor")
    return lax.ppermute(x, "tensor", [(j, j ^ 1) for j in range(tensor_count)])


def ring(x):
    tensor_count = lax.axis_size("tensor")
    rows = tensor_count // 2
    return lax.ppermute(
        x, "tensor", [(j, ((j // 2 + 1) % rows) * 2 + j % 2) for j in range(tensor_count)]
    )


def gather_tokens(x):
    tensor_count = lax.axis_size("tensor")
    rows = tensor_count // 2
    i = lax.axis_index("tensor")
    outer, inner = i // 2, i % 2
    own = [x]
    for _ in range(1, rows):
        own.append(ring(own[-1]))
    other = [partner(piece) for piece in own]
    steps = jnp.arange(rows)
    source = jnp.concatenate(
        [((outer - steps) % rows) * 2 + inner, ((outer - steps) % rows) * 2 + (1 - inner)]
    )
    return jnp.concatenate(own + other, axis=0), source


def scatter_tokens(partial, rider):
    tensor_count = lax.axis_size("tensor")
    rows = tensor_count // 2
    blocks = partial.reshape((2, rows, -1) + partial.shape[1:])
    mine = [
        blocks[0, s] + partner(blocks[1, s].astype(jnp.bfloat16)).astype(jnp.float32)
        for s in range(rows)
    ]
    carried = mine[1 % rows]
    for k in range(1, rows):
        if k == RELAY_STEP:
            carried, rider = lax.optimization_barrier((carried, rider))
        arrived = ring(carried.astype(jnp.bfloat16)).astype(jnp.float32)
        carried = arrived + mine[(k + 1) % rows]
    return carried, rider


def local(
    stretch,
    ln_gain,
    ln_bias,
    qkv_weight,
    qkv_bias,
    out_weight,
    out_bias,
    segment_ids,
    prefill_cache,
    block_dest,
):
    hidden = stretch.astype(jnp.float32)
    head_count = qkv_weight.shape[1] // (3 * HD)
    normed = normalize(hidden, ln_gain, ln_bias)
    gathered, source = gather_tokens(normed)
    split = split_heads(prefill_cache)
    gathered, split = lax.optimization_barrier((gathered, split))
    per_head_rows = lax.all_to_all(split, "tensor", split_axis=3, concat_axis=3, tiled=True)
    outgoing = send_decode(per_head_rows, block_dest)
    qkv = (
        jnp.dot(gathered, qkv_weight, preferred_element_type=jnp.float32) + qkv_bias
    ).astype(jnp.bfloat16)
    group_tokens = qkv.shape[0]
    place = (source[:, None] * normed.shape[0] + jnp.arange(normed.shape[0])[None, :]).reshape(-1)
    first_segment = segment_ids[0]
    segment_ids = segment_ids[place]
    heads = qkv.reshape(group_tokens, head_count, 3, HD)
    query = heads[:, :, 0]
    keys = heads[:, :, 1]
    value_rows = heads[:, :, 2]
    finished = per_head_rows[0]
    prefix_length = finished.shape[2] * finished.shape[3]
    cached_keys = finished[0].reshape(head_count, prefix_length, HD)
    old_values = finished[1].reshape(head_count, prefix_length, HD)
    scale = HD ** (-0.5)
    own_scores = jnp.einsum("qhd,khd->hqk", query, keys, preferred_element_type=jnp.float32) * scale
    old_scores = (
        jnp.einsum("qhd,hkd->hqk", query, cached_keys, preferred_element_type=jnp.float32) * scale
    )
    own_visible = (segment_ids[:, None] == segment_ids[None, :]) & (
        place[None, :] <= place[:, None]
    )
    old_visible = (segment_ids == first_segment)[:, None]
    own_scores = jnp.where(own_visible[None], own_scores, -jnp.inf)
    old_scores = jnp.where(old_visible[None], old_scores, -jnp.inf)
    scores = jnp.concatenate([old_scores, own_scores], axis=2)
    weights = jax.nn.softmax(scores, axis=-1).astype(jnp.bfloat16)
    context = jnp.einsum(
        "hqk,hkd->qhd",
        weights[:, :, :prefix_length],
        old_values,
        preferred_element_type=jnp.float32,
    )
    context = context + jnp.einsum(
        "hqk,khd->qhd",
        weights[:, :, prefix_length:],
        value_rows,
        preferred_element_type=jnp.float32,
    )
    context = context.astype(jnp.bfloat16).reshape(group_tokens, head_count * HD)
    decode_side_cache = receive_decode(outgoing)
    summed, decode_side_cache = scatter_tokens(
        jnp.dot(context, out_weight, preferred_element_type=jnp.float32), decode_side_cache
    )
    mixed = (hidden + summed + out_bias).astype(jnp.bfloat16)
    return (mixed, decode_side_cache)


def solution(mesh):
    return jax.shard_map(
        local,
        mesh=mesh,
        in_specs=(
            P(("pipe", "tensor"), None),
            P(),
            P(),
            P(None, "tensor"),
            P("tensor"),
            P("tensor", None),
            P(),
            P("pipe"),
            P(None, ("pipe", "tensor"), None, None, None),
            P(None, "pipe", None),
        ),
        out_specs=(P(("pipe", "tensor"), None), P(None, "pipe", None, None, "tensor")),
        check_vma=False,
    )
```

```python
import jax
import jax.numpy as jnp
from jax import lax
from jax.sharding import PartitionSpec as P

HD = 128
RELAY_STEP = 3
CACHE_STEP = 2


def normalize(x, gain, shift):
    mean = jnp.mean(x, axis=-1, keepdims=True)
    var = jnp.mean((x - mean) * (x - mean), axis=-1, keepdims=True)
    return ((x - mean) * lax.rsqrt(var + 1e-05) * gain + shift).astype(jnp.bfloat16)


def shifted(x, axis, k, n):
    return lax.ppermute(x, axis, [(j, (j + k) % n) for j in range(n)])


def split_heads(prefill_cache):
    tensor_count = lax.axis_size("tensor")
    layers, _, two, blk, width = prefill_cache.shape
    local_heads = width // tensor_count // HD
    split = prefill_cache.reshape(layers, two, blk, tensor_count, local_heads, HD)
    return jnp.transpose(split, (0, 1, 4, 3, 2, 5))


def send_decode(per_head_rows, block_dest):
    layers, two, local_heads, row_blocks, blk, _ = per_head_rows.shape
    pipe_count = lax.axis_size("pipe")
    capacity = 3 * row_blocks // (2 * pipe_count)
    dest = block_dest[:, :, 0]
    onehot = (dest[:, :, None] == jnp.arange(pipe_count, dtype=jnp.int32)[None, None, :]).astype(
        jnp.int32
    )
    earlier_tokens = jnp.cumsum(onehot, axis=1) - onehot
    slot = jnp.sum(earlier_tokens * onehot, axis=-1)
    position = dest * capacity + slot
    i = lax.axis_index("pipe")
    outgoing = []
    for k in range(pipe_count):
        targets = ((i + k) % pipe_count) * capacity + jnp.arange(capacity, dtype=jnp.int32)
        placement_index = (position[:, None, :] == targets[None, :, None]).astype(jnp.bfloat16)
        piece = jnp.einsum(
            "gud,gohdtc->guothc", placement_index, per_head_rows, preferred_element_type=jnp.float32
        ).astype(jnp.bfloat16)
        outgoing.append(piece.reshape((layers, capacity, two, blk, local_heads * HD)))
    return outgoing


def receive_decode(outgoing):
    pipe_count = lax.axis_size("pipe")
    i = lax.axis_index("pipe")
    layers, capacity = outgoing[0].shape[:2]
    arrived = jnp.zeros((layers, pipe_count * capacity) + outgoing[0].shape[2:], outgoing[0].dtype)
    for k in range(pipe_count):
        piece = outgoing[k] if k == 0 else shifted(outgoing[k], "pipe", k, pipe_count)
        arrived = lax.dynamic_update_slice_in_dim(
            arrived, piece, ((i - k) % pipe_count) * capacity, axis=1
        )
    return arrived

def partner(x):
    tensor_count = lax.axis_size("tensor")
    return lax.ppermute(x, "tensor", [(j, j ^ 1) for j in range(tensor_count)])


def ring(x):
    tensor_count = lax.axis_size("tensor")
    rows = tensor_count // 2
    return lax.ppermute(
        x, "tensor", [(j, ((j // 2 + 1) % rows) * 2 + j % 2) for j in range(tensor_count)]
    )


def gather_tokens(x, rider):
    tensor_count = lax.axis_size("tensor")
    rows = tensor_count // 2
    i = lax.axis_index("tensor")
    outer, inner = i // 2, i % 2
    own = [x]
    for k in range(1, rows):
        own.append(ring(own[-1]))
        if k == CACHE_STEP:
            own[-1], rider = lax.optimization_barrier((own[-1], rider))
    other = [partner(piece) for piece in own]
    steps = jnp.arange(rows)
    source = jnp.concatenate(
        [((outer - steps) % rows) * 2 + inner, ((outer - steps) % rows) * 2 + (1 - inner)]
    )
    return jnp.concatenate(own + other, axis=0), source, rider


def scatter_tokens(partial, rider):
    tensor_count = lax.axis_size("tensor")
    rows = tensor_count // 2
    blocks = partial.reshape((2, rows, -1) + partial.shape[1:])
    mine = [
        blocks[0, s] + partner(blocks[1, s].astype(jnp.bfloat16)).astype(jnp.float32)
        for s in range(rows)
    ]
    carried = mine[1 % rows]
    for k in range(1, rows):
        if k == RELAY_STEP:
            carried, rider = lax.optimization_barrier((carried, rider))
        arrived = ring(carried.astype(jnp.bfloat16)).astype(jnp.float32)
        carried = arrived + mine[(k + 1) % rows]
    return carried, rider


def local(
    stretch,
    ln_gain,
    ln_bias,
    qkv_weight,
    qkv_bias,
    out_weight,
    out_bias,
    segment_ids,
    prefill_cache,
    block_dest,
):
    hidden = stretch.astype(jnp.float32)
    head_count = qkv_weight.shape[1] // (3 * HD)
    normed = normalize(hidden, ln_gain, ln_bias)
    split = split_heads(prefill_cache)
    gathered, source, split = gather_tokens(normed, split)
    if CACHE_STEP == 0:
        gathered, split = lax.optimization_barrier((gathered, split))
    per_head_rows = lax.all_to_all(split, "tensor", split_axis=3, concat_axis=3, tiled=True)
    outgoing = send_decode(per_head_rows, block_dest)
    qkv = (
        jnp.dot(gathered, qkv_weight, preferred_element_type=jnp.float32) + qkv_bias
    ).astype(jnp.bfloat16)
    group_tokens = qkv.shape[0]
    place = (source[:, None] * normed.shape[0] + jnp.arange(normed.shape[0])[None, :]).reshape(-1)
    first_segment = segment_ids[0]
    segment_ids = segment_ids[place]
    heads = qkv.reshape(group_tokens, head_count, 3, HD)
    query = heads[:, :, 0]
    keys = heads[:, :, 1]
    value_rows = heads[:, :, 2]
    finished = per_head_rows[0]
    prefix_length = finished.shape[2] * finished.shape[3]
    cached_keys = finished[0].reshape(head_count, prefix_length, HD)
    old_values = finished[1].reshape(head_count, prefix_length, HD)
    scale = HD ** (-0.5)
    own_scores = jnp.einsum("qhd,khd->hqk", query, keys, preferred_element_type=jnp.float32) * scale
    old_scores = (
        jnp.einsum("qhd,hkd->hqk", query, cached_keys, preferred_element_type=jnp.float32) * scale
    )
    own_visible = (segment_ids[:, None] == segment_ids[None, :]) & (
        place[None, :] <= place[:, None]
    )
    old_visible = (segment_ids == first_segment)[:, None]
    own_scores = jnp.where(own_visible[None], own_scores, -jnp.inf)
    old_scores = jnp.where(old_visible[None], old_scores, -jnp.inf)
    scores = jnp.concatenate([old_scores, own_scores], axis=2)
    weights = jax.nn.softmax(scores, axis=-1).astype(jnp.bfloat16)
    context = jnp.einsum(
        "hqk,hkd->qhd",
        weights[:, :, :prefix_length],
        old_values,
        preferred_element_type=jnp.float32,
    )
    context = context + jnp.einsum(
        "hqk,khd->qhd",
        weights[:, :, prefix_length:],
        value_rows,
        preferred_element_type=jnp.float32,
    )
    context = context.astype(jnp.bfloat16).reshape(group_tokens, head_count * HD)
    decode_side_cache = receive_decode(outgoing)
    summed, decode_side_cache = scatter_tokens(
        jnp.dot(context, out_weight, preferred_element_type=jnp.float32), decode_side_cache
    )
    mixed = (hidden + summed + out_bias).astype(jnp.bfloat16)
    return (mixed, decode_side_cache)


def solution(mesh):
    return jax.shard_map(
        local,
        mesh=mesh,
        in_specs=(
            P(("pipe", "tensor"), None),
            P(),
            P(),
            P(None, "tensor"),
            P("tensor"),
            P("tensor", None),
            P(),
            P("pipe"),
            P(None, ("pipe", "tensor"), None, None, None),
            P(None, "pipe", None),
        ),
        out_specs=(P(("pipe", "tensor"), None), P(None, "pipe", None, None, "tensor")),
        check_vma=False,
    )
```

```python
import jax
import jax.numpy as jnp
from jax import lax
from jax.sharding import PartitionSpec as P

HD = 128
RELAY_STEP = 0
CACHE_STEP = 2
CHAIN_PARTNER = True


def normalize(x, gain, shift):
    mean = jnp.mean(x, axis=-1, keepdims=True)
    var = jnp.mean((x - mean) * (x - mean), axis=-1, keepdims=True)
    return ((x - mean) * lax.rsqrt(var + 1e-05) * gain + shift).astype(jnp.bfloat16)


def shifted(x, axis, k, n):
    return lax.ppermute(x, axis, [(j, (j + k) % n) for j in range(n)])


def split_heads(prefill_cache):
    tensor_count = lax.axis_size("tensor")
    layers, _, two, blk, width = prefill_cache.shape
    local_heads = width // tensor_count // HD
    split = prefill_cache.reshape(layers, two, blk, tensor_count, local_heads, HD)
    return jnp.transpose(split, (0, 1, 4, 3, 2, 5))


def send_decode(per_head_rows, block_dest):
    layers, two, local_heads, row_blocks, blk, _ = per_head_rows.shape
    pipe_count = lax.axis_size("pipe")
    capacity = 3 * row_blocks // (2 * pipe_count)
    dest = block_dest[:, :, 0]
    onehot = (dest[:, :, None] == jnp.arange(pipe_count, dtype=jnp.int32)[None, None, :]).astype(
        jnp.int32
    )
    earlier_tokens = jnp.cumsum(onehot, axis=1) - onehot
    slot = jnp.sum(earlier_tokens * onehot, axis=-1)
    position = dest * capacity + slot
    i = lax.axis_index("pipe")
    outgoing = []
    for k in range(pipe_count):
        targets = ((i + k) % pipe_count) * capacity + jnp.arange(capacity, dtype=jnp.int32)
        placement_index = (position[:, None, :] == targets[None, :, None]).astype(jnp.bfloat16)
        piece = jnp.einsum(
            "gud,gohdtc->guothc", placement_index, per_head_rows, preferred_element_type=jnp.float32
        ).astype(jnp.bfloat16)
        outgoing.append(piece.reshape((layers, capacity, two, blk, local_heads * HD)))
    return outgoing


def receive_decode(outgoing):
    pipe_count = lax.axis_size("pipe")
    i = lax.axis_index("pipe")
    layers, capacity = outgoing[0].shape[:2]
    arrived = jnp.zeros((layers, pipe_count * capacity) + outgoing[0].shape[2:], outgoing[0].dtype)
    for k in range(pipe_count):
        piece = outgoing[k] if k == 0 else shifted(outgoing[k], "pipe", k, pipe_count)
        arrived = lax.dynamic_update_slice_in_dim(
            arrived, piece, ((i - k) % pipe_count) * capacity, axis=1
        )
    return arrived

def partner(x):
    tensor_count = lax.axis_size("tensor")
    return lax.ppermute(x, "tensor", [(j, j ^ 1) for j in range(tensor_count)])


def ring(x):
    tensor_count = lax.axis_size("tensor")
    rows = tensor_count // 2
    return lax.ppermute(
        x, "tensor", [(j, ((j // 2 + 1) % rows) * 2 + j % 2) for j in range(tensor_count)]
    )


def gather_tokens(x, rider):
    tensor_count = lax.axis_size("tensor")
    rows = tensor_count // 2
    i = lax.axis_index("tensor")
    outer, inner = i // 2, i % 2
    own = [x]
    for k in range(1, rows):
        own.append(ring(own[-1]))
        if k == CACHE_STEP:
            own[-1], rider = lax.optimization_barrier((own[-1], rider))
    other = [partner(piece) for piece in own]
    steps = jnp.arange(rows)
    source = jnp.concatenate(
        [((outer - steps) % rows) * 2 + inner, ((outer - steps) % rows) * 2 + (1 - inner)]
    )
    return jnp.concatenate(own + other, axis=0), source, rider


def scatter_tokens(partial, rider):
    tensor_count = lax.axis_size("tensor")
    rows = tensor_count // 2
    blocks = partial.reshape((2, rows, -1) + partial.shape[1:])
    sent = blocks[1].astype(jnp.bfloat16)
    mine = [None] * rows
    previous = None
    for s in [(s + 1) % rows for s in range(rows)]:
        piece = sent[s]
        if previous is not None and CHAIN_PARTNER:
            piece, previous = lax.optimization_barrier((piece, previous))
        previous = partner(piece)
        mine[s] = blocks[0, s] + previous.astype(jnp.float32)
    carried = mine[1 % rows]
    for k in range(1, rows):
        if k == RELAY_STEP:
            carried, rider = lax.optimization_barrier((carried, rider))
        arrived = ring(carried.astype(jnp.bfloat16)).astype(jnp.float32)
        carried = arrived + mine[(k + 1) % rows]
    return carried, rider


def local(
    stretch,
    ln_gain,
    ln_bias,
    qkv_weight,
    qkv_bias,
    out_weight,
    out_bias,
    segment_ids,
    prefill_cache,
    block_dest,
):
    hidden = stretch.astype(jnp.float32)
    head_count = qkv_weight.shape[1] // (3 * HD)
    normed = normalize(hidden, ln_gain, ln_bias)
    split = split_heads(prefill_cache)
    gathered, source, split = gather_tokens(normed, split)
    if CACHE_STEP == 0:
        gathered, split = lax.optimization_barrier((gathered, split))
    per_head_rows = lax.all_to_all(split, "tensor", split_axis=3, concat_axis=3, tiled=True)
    outgoing = send_decode(per_head_rows, block_dest)
    qkv = (
        jnp.dot(gathered, qkv_weight, preferred_element_type=jnp.float32) + qkv_bias
    ).astype(jnp.bfloat16)
    group_tokens = qkv.shape[0]
    place = (source[:, None] * normed.shape[0] + jnp.arange(normed.shape[0])[None, :]).reshape(-1)
    first_segment = segment_ids[0]
    segment_ids = segment_ids[place]
    heads = qkv.reshape(group_tokens, head_count, 3, HD)
    query = heads[:, :, 0]
    keys = heads[:, :, 1]
    value_rows = heads[:, :, 2]
    finished = per_head_rows[0]
    prefix_length = finished.shape[2] * finished.shape[3]
    cached_keys = finished[0].reshape(head_count, prefix_length, HD)
    old_values = finished[1].reshape(head_count, prefix_length, HD)
    scale = HD ** (-0.5)
    own_scores = jnp.einsum("qhd,khd->hqk", query, keys, preferred_element_type=jnp.float32) * scale
    old_scores = (
        jnp.einsum("qhd,hkd->hqk", query, cached_keys, preferred_element_type=jnp.float32) * scale
    )
    own_visible = (segment_ids[:, None] == segment_ids[None, :]) & (
        place[None, :] <= place[:, None]
    )
    old_visible = (segment_ids == first_segment)[:, None]
    own_scores = jnp.where(own_visible[None], own_scores, -jnp.inf)
    old_scores = jnp.where(old_visible[None], old_scores, -jnp.inf)
    scores = jnp.concatenate([old_scores, own_scores], axis=2)
    weights = jax.nn.softmax(scores, axis=-1).astype(jnp.bfloat16)
    context = jnp.einsum(
        "hqk,hkd->qhd",
        weights[:, :, :prefix_length],
        old_values,
        preferred_element_type=jnp.float32,
    )
    context = context + jnp.einsum(
        "hqk,khd->qhd",
        weights[:, :, prefix_length:],
        value_rows,
        preferred_element_type=jnp.float32,
    )
    context = context.astype(jnp.bfloat16).reshape(group_tokens, head_count * HD)
    decode_side_cache = receive_decode(outgoing)
    summed, decode_side_cache = scatter_tokens(
        jnp.dot(context, out_weight, preferred_element_type=jnp.float32), decode_side_cache
    )
    mixed = (hidden + summed + out_bias).astype(jnp.bfloat16)
    return (mixed, decode_side_cache)


def solution(mesh):
    return jax.shard_map(
        local,
        mesh=mesh,
        in_specs=(
            P(("pipe", "tensor"), None),
            P(),
            P(),
            P(None, "tensor"),
            P("tensor"),
            P("tensor", None),
            P(),
            P("pipe"),
            P(None, ("pipe", "tensor"), None, None, None),
            P(None, "pipe", None),
        ),
        out_specs=(P(("pipe", "tensor"), None), P(None, "pipe", None, None, "tensor")),
        check_vma=False,
    )
```

```python
import jax
import jax.numpy as jnp
from jax import lax
from jax.sharding import PartitionSpec as P

HD = 128
RELAY_STEP = 0
CACHE_STEP = 2
CHAIN_PARTNER = True
CHAIN_RELAY = True


def normalize(x, gain, shift):
    mean = jnp.mean(x, axis=-1, keepdims=True)
    var = jnp.mean((x - mean) * (x - mean), axis=-1, keepdims=True)
    return ((x - mean) * lax.rsqrt(var + 1e-05) * gain + shift).astype(jnp.bfloat16)


def shifted(x, axis, k, n):
    return lax.ppermute(x, axis, [(j, (j + k) % n) for j in range(n)])


def split_heads(prefill_cache):
    tensor_count = lax.axis_size("tensor")
    layers, _, two, blk, width = prefill_cache.shape
    local_heads = width // tensor_count // HD
    split = prefill_cache.reshape(layers, two, blk, tensor_count, local_heads, HD)
    return jnp.transpose(split, (0, 1, 4, 3, 2, 5))


def send_decode(per_head_rows, block_dest):
    layers, two, local_heads, row_blocks, blk, _ = per_head_rows.shape
    pipe_count = lax.axis_size("pipe")
    capacity = 3 * row_blocks // (2 * pipe_count)
    dest = block_dest[:, :, 0]
    onehot = (dest[:, :, None] == jnp.arange(pipe_count, dtype=jnp.int32)[None, None, :]).astype(
        jnp.int32
    )
    earlier_tokens = jnp.cumsum(onehot, axis=1) - onehot
    slot = jnp.sum(earlier_tokens * onehot, axis=-1)
    position = dest * capacity + slot
    i = lax.axis_index("pipe")
    outgoing = []
    for k in range(pipe_count):
        targets = ((i + k) % pipe_count) * capacity + jnp.arange(capacity, dtype=jnp.int32)
        placement_index = (position[:, None, :] == targets[None, :, None]).astype(jnp.bfloat16)
        piece = jnp.einsum(
            "gud,gohdtc->guothc", placement_index, per_head_rows, preferred_element_type=jnp.float32
        ).astype(jnp.bfloat16)
        outgoing.append(piece.reshape((layers, capacity, two, blk, local_heads * HD)))
    return outgoing


def receive_decode(outgoing):
    pipe_count = lax.axis_size("pipe")
    i = lax.axis_index("pipe")
    layers, capacity = outgoing[0].shape[:2]
    arrived = jnp.zeros((layers, pipe_count * capacity) + outgoing[0].shape[2:], outgoing[0].dtype)
    previous = None
    for k in range(pipe_count):
        piece = outgoing[k]
        if k > 0:
            if previous is not None and CHAIN_RELAY:
                piece, previous = lax.optimization_barrier((piece, previous))
            piece = shifted(piece, "pipe", k, pipe_count)
            previous = piece
        arrived = lax.dynamic_update_slice_in_dim(
            arrived, piece, ((i - k) % pipe_count) * capacity, axis=1
        )
    return arrived

def partner(x):
    tensor_count = lax.axis_size("tensor")
    return lax.ppermute(x, "tensor", [(j, j ^ 1) for j in range(tensor_count)])


def ring(x):
    tensor_count = lax.axis_size("tensor")
    rows = tensor_count // 2
    return lax.ppermute(
        x, "tensor", [(j, ((j // 2 + 1) % rows) * 2 + j % 2) for j in range(tensor_count)]
    )


def gather_tokens(x, rider):
    tensor_count = lax.axis_size("tensor")
    rows = tensor_count // 2
    i = lax.axis_index("tensor")
    outer, inner = i // 2, i % 2
    own = [x]
    for k in range(1, rows):
        own.append(ring(own[-1]))
        if k == CACHE_STEP:
            own[-1], rider = lax.optimization_barrier((own[-1], rider))
    other = [partner(piece) for piece in own]
    steps = jnp.arange(rows)
    source = jnp.concatenate(
        [((outer - steps) % rows) * 2 + inner, ((outer - steps) % rows) * 2 + (1 - inner)]
    )
    return jnp.concatenate(own + other, axis=0), source, rider


def scatter_tokens(partial, rider):
    tensor_count = lax.axis_size("tensor")
    rows = tensor_count // 2
    blocks = partial.reshape((2, rows, -1) + partial.shape[1:])
    sent = blocks[1].astype(jnp.bfloat16)
    mine = [None] * rows
    previous = None
    for s in [(s + 1) % rows for s in range(rows)]:
        piece = sent[s]
        if previous is not None and CHAIN_PARTNER:
            piece, previous = lax.optimization_barrier((piece, previous))
        previous = partner(piece)
        mine[s] = blocks[0, s] + previous.astype(jnp.float32)
    carried = mine[1 % rows]
    for k in range(1, rows):
        if k == RELAY_STEP:
            carried, rider = lax.optimization_barrier((carried, rider))
        arrived = ring(carried.astype(jnp.bfloat16)).astype(jnp.float32)
        carried = arrived + mine[(k + 1) % rows]
    return carried, rider


def local(
    stretch,
    ln_gain,
    ln_bias,
    qkv_weight,
    qkv_bias,
    out_weight,
    out_bias,
    segment_ids,
    prefill_cache,
    block_dest,
):
    hidden = stretch.astype(jnp.float32)
    head_count = qkv_weight.shape[1] // (3 * HD)
    normed = normalize(hidden, ln_gain, ln_bias)
    split = split_heads(prefill_cache)
    gathered, source, split = gather_tokens(normed, split)
    if CACHE_STEP == 0:
        gathered, split = lax.optimization_barrier((gathered, split))
    per_head_rows = lax.all_to_all(split, "tensor", split_axis=3, concat_axis=3, tiled=True)
    outgoing = send_decode(per_head_rows, block_dest)
    qkv = (
        jnp.dot(gathered, qkv_weight, preferred_element_type=jnp.float32) + qkv_bias
    ).astype(jnp.bfloat16)
    group_tokens = qkv.shape[0]
    place = (source[:, None] * normed.shape[0] + jnp.arange(normed.shape[0])[None, :]).reshape(-1)
    first_segment = segment_ids[0]
    segment_ids = segment_ids[place]
    heads = qkv.reshape(group_tokens, head_count, 3, HD)
    query = heads[:, :, 0]
    keys = heads[:, :, 1]
    value_rows = heads[:, :, 2]
    finished = per_head_rows[0]
    prefix_length = finished.shape[2] * finished.shape[3]
    cached_keys = finished[0].reshape(head_count, prefix_length, HD)
    old_values = finished[1].reshape(head_count, prefix_length, HD)
    scale = HD ** (-0.5)
    own_scores = jnp.einsum("qhd,khd->hqk", query, keys, preferred_element_type=jnp.float32) * scale
    old_scores = (
        jnp.einsum("qhd,hkd->hqk", query, cached_keys, preferred_element_type=jnp.float32) * scale
    )
    own_visible = (segment_ids[:, None] == segment_ids[None, :]) & (
        place[None, :] <= place[:, None]
    )
    old_visible = (segment_ids == first_segment)[:, None]
    own_scores = jnp.where(own_visible[None], own_scores, -jnp.inf)
    old_scores = jnp.where(old_visible[None], old_scores, -jnp.inf)
    scores = jnp.concatenate([old_scores, own_scores], axis=2)
    weights = jax.nn.softmax(scores, axis=-1).astype(jnp.bfloat16)
    context = jnp.einsum(
        "hqk,hkd->qhd",
        weights[:, :, :prefix_length],
        old_values,
        preferred_element_type=jnp.float32,
    )
    context = context + jnp.einsum(
        "hqk,khd->qhd",
        weights[:, :, prefix_length:],
        value_rows,
        preferred_element_type=jnp.float32,
    )
    context = context.astype(jnp.bfloat16).reshape(group_tokens, head_count * HD)
    decode_side_cache = receive_decode(outgoing)
    summed, decode_side_cache = scatter_tokens(
        jnp.dot(context, out_weight, preferred_element_type=jnp.float32), decode_side_cache
    )
    mixed = (hidden + summed + out_bias).astype(jnp.bfloat16)
    return (mixed, decode_side_cache)


def solution(mesh):
    return jax.shard_map(
        local,
        mesh=mesh,
        in_specs=(
            P(("pipe", "tensor"), None),
            P(),
            P(),
            P(None, "tensor"),
            P("tensor"),
            P("tensor", None),
            P(),
            P("pipe"),
            P(None, ("pipe", "tensor"), None, None, None),
            P(None, "pipe", None),
        ),
        out_specs=(P(("pipe", "tensor"), None), P(None, "pipe", None, None, "tensor")),
        check_vma=False,
    )
```

```python
import jax
import jax.numpy as jnp
from jax import lax
from jax.sharding import PartitionSpec as P

HD = 128
RELAY_STEP = 0
CACHE_STEP = 2
CHAIN_PARTNER = True
CHAIN_RELAY = True


def normalize(x, gain, shift):
    mean = jnp.mean(x, axis=-1, keepdims=True)
    var = jnp.mean((x - mean) * (x - mean), axis=-1, keepdims=True)
    return ((x - mean) * lax.rsqrt(var + 1e-05) * gain + shift).astype(jnp.bfloat16)


def shifted(x, axis, k, n):
    return lax.ppermute(x, axis, [(j, (j + k) % n) for j in range(n)])


def split_heads(prefill_cache):
    tensor_count = lax.axis_size("tensor")
    layers, _, two, blk, width = prefill_cache.shape
    local_heads = width // tensor_count // HD
    split = prefill_cache.reshape(layers, two, blk, tensor_count, local_heads, HD)
    return jnp.transpose(split, (0, 1, 4, 3, 2, 5))


def send_decode(per_head_rows, block_dest):
    layers, two, local_heads, row_blocks, blk, _ = per_head_rows.shape
    pipe_count = lax.axis_size("pipe")
    capacity = 3 * row_blocks // (2 * pipe_count)
    dest = block_dest[:, :, 0]
    onehot = (dest[:, :, None] == jnp.arange(pipe_count, dtype=jnp.int32)[None, None, :]).astype(
        jnp.int32
    )
    earlier_tokens = jnp.cumsum(onehot, axis=1) - onehot
    slot = jnp.sum(earlier_tokens * onehot, axis=-1)
    position = dest * capacity + slot
    i = lax.axis_index("pipe")
    outgoing = []
    for k in range(pipe_count):
        targets = ((i + k) % pipe_count) * capacity + jnp.arange(capacity, dtype=jnp.int32)
        placement_index = (position[:, None, :] == targets[None, :, None]).astype(jnp.bfloat16)
        piece = jnp.einsum(
            "gud,gohdtc->guothc", placement_index, per_head_rows, preferred_element_type=jnp.float32
        ).astype(jnp.bfloat16)
        outgoing.append(piece.reshape((layers, capacity, two, blk, local_heads * HD)))
    return outgoing


def receive_decode(outgoing):
    pipe_count = lax.axis_size("pipe")
    i = lax.axis_index("pipe")
    layers, capacity = outgoing[0].shape[:2]
    arrived = jnp.zeros((layers, pipe_count * capacity) + outgoing[0].shape[2:], outgoing[0].dtype)
    previous = None
    for k in range(pipe_count):
        piece = outgoing[k]
        if k > 0:
            if previous is not None and CHAIN_RELAY:
                piece, previous = lax.optimization_barrier((piece, previous))
            piece = shifted(piece, "pipe", k, pipe_count)
            previous = piece
        arrived = lax.dynamic_update_slice_in_dim(
            arrived, piece, ((i - k) % pipe_count) * capacity, axis=1
        )
    return arrived

def partner(x):
    tensor_count = lax.axis_size("tensor")
    return lax.ppermute(x, "tensor", [(j, j ^ 1) for j in range(tensor_count)])


def ring(x):
    tensor_count = lax.axis_size("tensor")
    rows = tensor_count // 2
    return lax.ppermute(
        x, "tensor", [(j, ((j // 2 + 1) % rows) * 2 + j % 2) for j in range(tensor_count)]
    )


def gather_tokens(x, rider):
    tensor_count = lax.axis_size("tensor")
    rows = tensor_count // 2
    i = lax.axis_index("tensor")
    outer, inner = i // 2, i % 2
    own = [x]
    for k in range(1, rows):
        own.append(ring(own[-1]))
        if k == CACHE_STEP:
            own[-1], rider = lax.optimization_barrier((own[-1], rider))
    other = [partner(piece) for piece in own]
    steps = jnp.arange(rows)
    source = jnp.concatenate(
        [((outer - steps) % rows) * 2 + inner, ((outer - steps) % rows) * 2 + (1 - inner)]
    )
    return jnp.concatenate(own + other, axis=0), source, rider


def scatter_tokens(partial, rider):
    tensor_count = lax.axis_size("tensor")
    rows = tensor_count // 2
    kept = partial[0].reshape((rows, -1) + partial[0].shape[1:])
    sent = partial[1].astype(jnp.bfloat16).reshape((rows, -1) + partial[1].shape[1:])
    mine = [None] * rows
    previous = None
    for s in [(s + 1) % rows for s in range(rows)]:
        piece = sent[s]
        if previous is not None and CHAIN_PARTNER:
            piece, previous = lax.optimization_barrier((piece, previous))
        previous = partner(piece)
        mine[s] = kept[s] + previous.astype(jnp.float32)
    carried = mine[1 % rows]
    for k in range(1, rows):
        if k == RELAY_STEP:
            carried, rider = lax.optimization_barrier((carried, rider))
        arrived = ring(carried.astype(jnp.bfloat16)).astype(jnp.float32)
        carried = arrived + mine[(k + 1) % rows]
    return carried, rider


def local(
    stretch,
    ln_gain,
    ln_bias,
    qkv_weight,
    qkv_bias,
    out_weight,
    out_bias,
    segment_ids,
    prefill_cache,
    block_dest,
):
    hidden = stretch.astype(jnp.float32)
    head_count = qkv_weight.shape[1] // (3 * HD)
    normed = normalize(hidden, ln_gain, ln_bias)
    split = split_heads(prefill_cache)
    gathered, source, split = gather_tokens(normed, split)
    if CACHE_STEP == 0:
        gathered, split = lax.optimization_barrier((gathered, split))
    per_head_rows = lax.all_to_all(split, "tensor", split_axis=3, concat_axis=3, tiled=True)
    outgoing = send_decode(per_head_rows, block_dest)
    qkv = (
        jnp.dot(gathered, qkv_weight, preferred_element_type=jnp.float32) + qkv_bias
    ).astype(jnp.bfloat16)
    group_tokens = qkv.shape[0]
    place = (source[:, None] * normed.shape[0] + jnp.arange(normed.shape[0])[None, :]).reshape(-1)
    first_segment = segment_ids[0]
    segment_ids = segment_ids[place]
    heads = qkv.reshape(group_tokens, head_count, 3, HD)
    query = heads[:, :, 0]
    keys = heads[:, :, 1]
    value_rows = heads[:, :, 2]
    finished = per_head_rows[0]
    prefix_length = finished.shape[2] * finished.shape[3]
    cached_keys = finished[0].reshape(head_count, prefix_length, HD)
    old_values = finished[1].reshape(head_count, prefix_length, HD)
    scale = HD ** (-0.5)
    own_scores = jnp.einsum("qhd,khd->hqk", query, keys, preferred_element_type=jnp.float32) * scale
    old_scores = (
        jnp.einsum("qhd,hkd->hqk", query, cached_keys, preferred_element_type=jnp.float32) * scale
    )
    own_visible = (segment_ids[:, None] == segment_ids[None, :]) & (
        place[None, :] <= place[:, None]
    )
    old_visible = (segment_ids == first_segment)[:, None]
    own_scores = jnp.where(own_visible[None], own_scores, -jnp.inf)
    old_scores = jnp.where(old_visible[None], old_scores, -jnp.inf)
    scores = jnp.concatenate([old_scores, own_scores], axis=2)
    weights = jax.nn.softmax(scores, axis=-1).astype(jnp.bfloat16)
    context = jnp.einsum(
        "hqk,hkd->qhd",
        weights[:, :, :prefix_length],
        old_values,
        preferred_element_type=jnp.float32,
    )
    context = context + jnp.einsum(
        "hqk,khd->qhd",
        weights[:, :, prefix_length:],
        value_rows,
        preferred_element_type=jnp.float32,
    )
    context = context.astype(jnp.bfloat16).reshape(group_tokens, head_count * HD)
    decode_side_cache = receive_decode(outgoing)
    half = context.shape[0] // 2
    summed, decode_side_cache = scatter_tokens(
        [
            jnp.dot(context[:half], out_weight, preferred_element_type=jnp.float32),
            jnp.dot(context[half:], out_weight, preferred_element_type=jnp.bfloat16),
        ],
        decode_side_cache,
    )
    mixed = (hidden + summed + out_bias).astype(jnp.bfloat16)
    return (mixed, decode_side_cache)


def solution(mesh):
    return jax.shard_map(
        local,
        mesh=mesh,
        in_specs=(
            P(("pipe", "tensor"), None),
            P(),
            P(),
            P(None, "tensor"),
            P("tensor"),
            P("tensor", None),
            P(),
            P("pipe"),
            P(None, ("pipe", "tensor"), None, None, None),
            P(None, "pipe", None),
        ),
        out_specs=(P(("pipe", "tensor"), None), P(None, "pipe", None, None, "tensor")),
        check_vma=False,
    )
```
